256 devices in a mesh: tm: 16 (over y_lo, z), chan: 16 (over y_hi, x, core).
Axes of the slice: x: 4, y: 4 (y_hi: 2, y_lo: 2; y = y_hi * 2 + y_lo), z: 8, core: 2. Of those that a mesh axis runs over, the one named last changes fastest.
Arguments:
- record: bfloat16 [5120, 16384], P('chan', 'tm'), may hold values from -200 to 200
- owner: int32 [4], replicated, may hold values from 0 to 15, as said below
- offsets: int32 [4, 16], replicated, may hold values from 0 to 924
Outputs:
- score: float32 [4, 16, 16384], P(None, None, 'tm')
The draws below stay inside these ranges and needn't reach their ends.
Inputs may be any that keep to these rules, and one draw needn't show every extreme that they name: `owner`: no two batches share a time block, and one batch is always held by the last block. `offsets`: a template lies wholly inside its owner's block.
All inputs are finite; a program needn't handle non-finite values.
Results may differ from the reference program's by a relative error of at most 0.0003.
Values may be sent and summed in bfloat16 or wider, within the bound.
No kernel may reach another device: no remote copies, remote signals or barrier semaphores. Data moves between devices by JAX's collectives and lax.ppermute only.
A program may use at most 64 MiB of HBM per device.

```python
import jax
import jax.numpy as jnp
from jax import lax

TDEV = 1024
L = 100
K = 16
NB = 4
CHANNELS = 5120
SAMPLES = 16384
N_TM = 16


def draw_record(key, part):
    keys = jax.random.split(key, 4)
    position = jnp.arange(CHANNELS, dtype=jnp.float32) / CHANNELS
    spread = 0.7
    noise = jax.random.normal(keys[0], (CHANNELS, SAMPLES), jnp.float32)
    gain = jnp.exp(0.55 * position + jax.random.uniform(keys[1], (CHANNELS,), jnp.float32, -spread, spread))
    wave = jax.random.normal(keys[2], (SAMPLES,), jnp.float32)
    pace = jnp.exp(jax.random.uniform(keys[3], (SAMPLES,), jnp.float32, -0.5, 0.5))
    values = gain[:, None] * pace[None, :] * (0.8 * wave[None, :] + noise)
    return jnp.clip(values, -200.0, 200.0).astype(jnp.bfloat16)


def draw_owner(key, part):
    others = jax.random.permutation(jax.random.fold_in(key, 11), N_TM - 1)[:NB - 1].astype(jnp.int32)
    chosen = jnp.concatenate([others, jnp.full((1,), N_TM - 1, jnp.int32)])
    order = jax.random.permutation(jax.random.fold_in(key, 12), NB)
    return chosen[order].astype(jnp.int32)


def set_ends(entries, rng, least, high):
    place = [jax.random.randint(jax.random.fold_in(rng, axis), (), 0, length) for axis, length in enumerate(entries.shape)]
    longest = entries.shape.index(max(entries.shape))
    next_to = place[:longest] + [(place[longest] + 1) % entries.shape[longest]] + place[longest + 1:]
    return entries.at[tuple(place)].set(least).at[tuple(next_to)].set(high)


def setup_inputs(seed: int = 0) -> dict:
    splits = jax.random.split(jax.random.key(seed), 4)
    record = draw_record(jax.random.fold_in(splits[3], 71), 0)
    owner = draw_owner(jax.random.fold_in(splits[3], 71), 0)
    offsets = set_ends(jax.random.randint(splits[2], (NB, K), 0, TDEV - L + 1), jax.random.fold_in(splits[2], 1), 0, TDEV - L).astype(jnp.int32)
    return dict(record=record, owner=owner, offsets=offsets)


def reference(record, owner, offsets):
    full = record.astype(jnp.float32)
    starts = (owner[:, None] * TDEV + offsets).reshape(-1).astype(jnp.int32)
    windows = jax.vmap(lambda s: lax.dynamic_slice_in_dim(full, s, L, 1))(starts)
    padded = jnp.pad(full, ((0, 0), (0, L - 1)))

    def tap_step(j, acc):
        weights = lax.dynamic_index_in_dim(windows, j, 2, keepdims=False)
        shifted = lax.dynamic_slice_in_dim(padded, j, SAMPLES, 1)
        return acc + jnp.dot(weights, shifted, preferred_element_type=jnp.float32, precision=lax.Precision.HIGHEST)
    corr = lax.fori_loop(0, L, tap_step, jnp.zeros((NB * K, SAMPLES), jnp.float32))
    squares = lax.optimization_barrier(jnp.sum(padded * padded, axis=0))
    running = jnp.concatenate([jnp.zeros((1,), jnp.float32), jnp.cumsum(squares)])
    energy = running[L:L + SAMPLES] - running[:SAMPLES]
    tnorm = lax.optimization_barrier(jnp.sum(windows * windows, axis=(1, 2)))
    score = corr / jnp.sqrt((energy[None, :] + 1e-05) * tnorm[:, None])
    return score.reshape(NB, K, SAMPLES)
```

```python
import jax
import jax.numpy as jnp
from jax import lax
from jax.sharding import PartitionSpec as P

L = 100


def from_behind(value, axis, by):
    peers = lax.axis_size(axis)
    pairs = [(i, i + by) for i in range(peers) if 0 <= i + by < peers]
    return lax.ppermute(value, axis, pairs)


def dense_pieces(block, peers):
    size = block.size // peers
    return block.reshape(peers, 16, size // 16)


def owner_blocks(record, owner, axis):
    peers = lax.axis_size(axis)
    width, samples = record.shape
    batches = owner.shape[0]
    pieces = dense_pieces(record, peers)
    got = lax.all_to_all(pieces, axis, 0, 0, tiled=False)
    sel = jnp.stack([lax.dynamic_index_in_dim(got, owner[b], 0, keepdims=False) for b in range(batches)])
    rep = jnp.broadcast_to(sel[None], (peers,) + sel.shape)
    recv = lax.all_to_all(rep, axis, 0, 0, tiled=False)
    return jnp.swapaxes(recv, 0, 1).reshape(batches, width, samples)


def cut_windows(blocks, offsets, taps):
    batches, per_batch = offsets.shape
    _, width, samples = blocks.shape
    idx = (offsets[:, :, None] + jnp.arange(taps, dtype=offsets.dtype)[None, None, :]).reshape(batches, per_batch * taps)
    hot = (jnp.arange(samples, dtype=offsets.dtype)[None, :, None] == idx[:, None, :]).astype(blocks.dtype)
    cut = jnp.einsum("bcs,bsn->bcn", blocks, hot, preferred_element_type=jnp.float32).astype(blocks.dtype)
    cut = cut.reshape(batches, width, per_batch, taps)
    return jnp.transpose(cut, (0, 2, 1, 3)).reshape(batches * per_batch, width, taps)


def chan_sum(x, axis):
    peers = lax.axis_size(axis)
    shape = x.shape
    pieces = dense_pieces(x, peers)
    got = lax.all_to_all(pieces, axis, 0, 0, tiled=False)
    mine = jnp.sum(got, axis=0)
    rep = jnp.broadcast_to(mine[None], (peers,) + mine.shape)
    back = lax.all_to_all(rep, axis, 0, 0, tiled=False)
    return back.reshape(shape)


def on_device(record, owner, offsets):
    width, samples = record.shape
    batches, per_batch = offsets.shape
    taps = L
    templates = batches * per_batch
    rim = from_behind(record[:, : taps - 1], "tm", -1)
    extended = jnp.concatenate([record, rim], axis=1)
    blocks = owner_blocks(record, owner, "tm")
    weights = cut_windows(blocks, offsets, taps)
    corr_part = lax.conv_general_dilated(
        extended[None], weights, (1,), "VALID",
        dimension_numbers=("NCH", "OIH", "NCH"), preferred_element_type=jnp.float32,
    )[0]
    widened = extended.astype(jnp.float32)
    squares = jnp.sum(widened * widened, axis=0)
    running = jnp.concatenate([jnp.zeros((1,), jnp.float32), jnp.cumsum(squares)])
    energy_part = running[taps : taps + samples] - running[:samples]
    floats = weights.astype(jnp.float32)
    tnorm_part = jnp.sum(floats * floats, axis=(1, 2))
    rows = 80
    packed = jnp.zeros((rows, samples), jnp.float32)
    packed = packed.at[:templates].set(corr_part)
    packed = packed.at[templates].set(energy_part)
    packed = packed.at[templates + 1, :templates].set(tnorm_part)
    total = chan_sum(packed, "chan")
    corr = total[:templates]
    energy = total[templates]
    tnorm = total[templates + 1, :templates]
    score = corr / jnp.sqrt((energy[None, :] + 1e-05) * tnorm[:, None])
    return score.reshape(batches, per_batch, samples)


def solution(mesh):
    in_specs = (P("chan", "tm"), P(), P())
    out_specs = P(None, None, "tm")
    return jax.shard_map(
        on_device, mesh=mesh, in_specs=in_specs, out_specs=out_specs, check_vma=False
    )
```

```python
import jax
import jax.numpy as jnp
from jax import lax
from jax.sharding import PartitionSpec as P

L = 100
PHASES = 4


def from_behind(value, axis, by):
    peers = lax.axis_size(axis)
    pairs = [(i, i + by) for i in range(peers) if 0 <= i + by < peers]
    return lax.ppermute(value, axis, pairs)


def dense_pieces(block, peers):
    size = block.size // peers
    return block.reshape(peers, 16, size // 16)


def owner_blocks(record, owner, axis):
    peers = lax.axis_size(axis)
    width, samples = record.shape
    batches = owner.shape[0]
    pieces = dense_pieces(record, peers)
    got = lax.all_to_all(pieces, axis, 0, 0, tiled=False)
    sel = jnp.stack([lax.dynamic_index_in_dim(got, owner[b], 0, keepdims=False) for b in range(batches)])
    rep = jnp.broadcast_to(sel[None], (peers,) + sel.shape)
    recv = lax.all_to_all(rep, axis, 0, 0, tiled=False)
    return jnp.swapaxes(recv, 0, 1).reshape(batches, width, samples)


def cut_windows(blocks, offsets, taps, phases):
    batches, per_batch = offsets.shape
    _, width, samples = blocks.shape
    steps = taps // phases
    lag = jnp.arange(taps, dtype=offsets.dtype).reshape(steps, phases)
    idx = offsets[:, :, None, None] + lag[None, None]
    hot = (jnp.arange(samples, dtype=offsets.dtype) == idx[..., None]).astype(blocks.dtype)
    cut = jnp.einsum("bkips,bcs->ibkpc", hot, blocks, preferred_element_type=jnp.float32).astype(blocks.dtype)
    return cut.reshape(steps, batches * per_batch * phases, width)


def window_norms(blocks, offsets, taps):
    floats = blocks.astype(jnp.float32)
    column = jnp.sum(floats * floats, axis=1)
    samples = blocks.shape[2]
    at = jnp.arange(samples, dtype=offsets.dtype)
    inside = (at >= offsets[:, :, None]) & (at < offsets[:, :, None] + taps)
    return jnp.sum(jnp.where(inside, column[:, None, :], 0.0), axis=2).reshape(-1)


def chan_sum(x, axis):
    peers = lax.axis_size(axis)
    shape = x.shape
    pieces = dense_pieces(x, peers)
    got = lax.all_to_all(pieces, axis, 0, 0, tiled=False)
    mine = jnp.sum(got, axis=0)
    rep = jnp.broadcast_to(mine[None], (peers,) + mine.shape)
    back = lax.all_to_all(rep, axis, 0, 0, tiled=False)
    return back.reshape(shape)


def on_device(record, owner, offsets):
    width, samples = record.shape
    batches, per_batch = offsets.shape
    taps = L
    templates = batches * per_batch
    rim = from_behind(record[:, : taps - 1], "tm", -1)
    extended = jnp.concatenate([record, rim], axis=1)
    blocks = owner_blocks(record, owner, "tm")
    phases = PHASES
    weights = cut_windows(blocks, offsets, taps, phases)
    out = lax.conv_general_dilated(
        extended[None], weights, (1,), "VALID", rhs_dilation=(phases,),
        dimension_numbers=("NCH", "HOI", "NCH"), preferred_element_type=jnp.float32,
    )[0]
    out = out.reshape(templates, phases, out.shape[-1])
    corr_part = out[:, 0, :samples]
    for p in range(1, phases):
        corr_part = corr_part + out[:, p, p : p + samples]
    widened = extended.astype(jnp.float32)
    squares = jnp.sum(widened * widened, axis=0)
    running = jnp.concatenate([jnp.zeros((1,), jnp.float32), jnp.cumsum(squares)])
    energy_part = running[taps : taps + samples] - running[:samples]
    tnorm_part = window_norms(blocks, offsets, taps)
    rows = 80
    packed = jnp.zeros((rows, samples), jnp.float32)
    packed = packed.at[:templates].set(corr_part)
    packed = packed.at[templates].set(energy_part)
    packed = packed.at[templates + 1, :templates].set(tnorm_part)
    total = chan_sum(packed, "chan")
    corr = total[:templates]
    energy = total[templates]
    tnorm = total[templates + 1, :templates]
    score = corr / jnp.sqrt((energy[None, :] + 1e-05) * tnorm[:, None])
    return score.reshape(batches, per_batch, samples)


def solution(mesh):
    in_specs = (P("chan", "tm"), P(), P())
    out_specs = P(None, None, "tm")
    return jax.shard_map(
        on_device, mesh=mesh, in_specs=in_specs, out_specs=out_specs, check_vma=False
    )
```

```python
import jax
import jax.numpy as jnp
from jax import lax
from jax.sharding import PartitionSpec as P

L = 100
PHASES = 4
STAGES = 1


def from_behind(value, axis, by):
    peers = lax.axis_size(axis)
    pairs = [(i, i + by) for i in range(peers) if 0 <= i + by < peers]
    return lax.ppermute(value, axis, pairs)


def dense_pieces(block, peers):
    size = block.size // peers
    return block.reshape(peers, size // 128, 128)


def scatter_owners(record, owner, axis):
    peers = lax.axis_size(axis)
    pieces = dense_pieces(record, peers)
    got = lax.all_to_all(pieces, axis, 0, 0, tiled=False)
    return jnp.stack([lax.dynamic_index_in_dim(got, owner[b], 0, keepdims=False) for b in range(owner.shape[0])])


def gather_blocks(sel, axis, shape):
    peers = lax.axis_size(axis)
    rep = jnp.broadcast_to(sel[None], (peers,) + sel.shape)
    recv = lax.all_to_all(rep, axis, 0, 0, tiled=False)
    return jnp.swapaxes(recv, 0, 1).reshape((sel.shape[0],) + shape)


def cut_windows(blocks, offsets, taps, span, phases):
    batches, per_batch = offsets.shape
    _, width, samples = blocks.shape
    steps = span // phases
    lag = jnp.arange(span, dtype=offsets.dtype).reshape(steps, phases)
    idx = offsets[:, :, None, None] + lag[None, None]
    hot = (jnp.arange(samples, dtype=offsets.dtype) == idx[..., None]) & (lag[None, None, :, :, None] < taps)
    hot = hot.astype(blocks.dtype)
    cut = jnp.einsum("bkips,bcs->ibkpc", hot, blocks, preferred_element_type=jnp.float32).astype(blocks.dtype)
    return cut.reshape(steps, batches * per_batch * phases, width)


def window_norms(blocks, offsets, taps):
    floats = blocks.astype(jnp.float32)
    column = jnp.sum(floats * floats, axis=1)
    samples = blocks.shape[2]
    at = jnp.arange(samples, dtype=offsets.dtype)
    inside = (at >= offsets[:, :, None]) & (at < offsets[:, :, None] + taps)
    return jnp.sum(jnp.where(inside, column[:, None, :], 0.0), axis=2).reshape(-1)


def chan_sum(x, axis):
    peers = lax.axis_size(axis)
    shape = x.shape
    pieces = dense_pieces(x, peers)
    got = lax.all_to_all(pieces, axis, 0, 0, tiled=False)
    mine = jnp.sum(got, axis=0)
    rep = jnp.broadcast_to(mine[None], (peers,) + mine.shape)
    back = lax.all_to_all(rep, axis, 0, 0, tiled=False)
    return back.reshape(shape)


def correlate(extended, weights, phases, count, samples):
    out = lax.conv_general_dilated(
        extended[None], weights, (1,), "VALID", rhs_dilation=(phases,),
        dimension_numbers=("NCH", "HOI", "NCH"), preferred_element_type=jnp.float32,
    )[0]
    out = out.reshape(count, phases, out.shape[-1])
    corr = out[:, 0, :samples]
    for p in range(1, phases):
        corr = corr + out[:, p, p : p + samples]
    return corr


def on_device(record, owner, offsets):
    width, samples = record.shape
    batches, per_batch = offsets.shape
    taps = L
    templates = batches * per_batch
    phases = PHASES
    span = -(-taps // phases) * phases
    rim = from_behind(record[:, : taps - 1], "tm", -1)
    rim, record = lax.optimization_barrier((rim, record))
    extended = jnp.concatenate(
        [record, rim, jnp.zeros((width, span - taps), record.dtype)], axis=1
    )
    widened = extended[:, : samples + taps - 1].astype(jnp.float32)
    squares = jnp.sum(widened * widened, axis=0)
    running = jnp.concatenate([jnp.zeros((1,), jnp.float32), jnp.cumsum(squares)])
    energy_part = running[taps : taps + samples] - running[:samples]
    sel = scatter_owners(record, owner, "tm")
    step = batches // STAGES
    corrs = []
    norms = []
    for g in range(STAGES):
        part = slice(g * step, (g + 1) * step)
        blocks = gather_blocks(sel[part], "tm", (width, samples))
        weights = cut_windows(blocks, offsets[part], taps, span, phases)
        corrs.append(correlate(extended, weights, phases, step * per_batch, samples))
        norms.append(window_norms(blocks, offsets[part], taps))
    rows = 80
    packed = jnp.zeros((rows, samples), jnp.float32)
    packed = packed.at[:templates].set(jnp.concatenate(corrs, axis=0))
    packed = packed.at[templates].set(energy_part)
    packed = packed.at[templates + 1, :templates].set(jnp.concatenate(norms))
    total = chan_sum(packed, "chan")
    corr = total[:templates]
    energy = total[templates]
    tnorm = total[templates + 1, :templates]
    score = corr / jnp.sqrt((energy[None, :] + 1e-05) * tnorm[:, None])
    return score.reshape(batches, per_batch, samples)


def solution(mesh):
    in_specs = (P("chan", "tm"), P(), P())
    out_specs = P(None, None, "tm")
    return jax.shard_map(
        on_device, mesh=mesh, in_specs=in_specs, out_specs=out_specs, check_vma=False
    )
```

```python
import jax
import jax.numpy as jnp
from jax import lax
from jax.sharding import PartitionSpec as P

L = 100
PHASES = 4
STAGES = 1
BLOCK_GRID = (4, 4)
SUM_GRID = (2, 8)


def from_behind(value, axis, by):
    peers = lax.axis_size(axis)
    pairs = [(i, i + by) for i in range(peers) if 0 <= i + by < peers]
    return lax.ppermute(value, axis, pairs)


def dense_pieces(block, across):
    down = block.shape[0] // across[0]
    wide = block.shape[1] // across[1]
    grid = block.reshape(across[0], down, across[1], wide)
    return jnp.transpose(grid, (0, 2, 1, 3)).reshape(across[0] * across[1], down, wide)


def join_pieces(pieces, across):
    _, *middle, down, wide = pieces.shape
    grid = pieces.reshape(across[0], across[1], *middle, down, wide)
    lead = len(middle)
    order = tuple(range(2, 2 + lead)) + (0, 2 + lead, 1, 3 + lead)
    return jnp.transpose(grid, order).reshape(*middle, across[0] * down, across[1] * wide)


def scatter_owners(record, owner, axis):
    pieces = dense_pieces(record, BLOCK_GRID)
    got = lax.all_to_all(pieces, axis, 0, 0, tiled=False)
    return jnp.stack([lax.dynamic_index_in_dim(got, owner[b], 0, keepdims=False) for b in range(owner.shape[0])])


def gather_blocks(sel, axis, shape):
    peers = lax.axis_size(axis)
    rep = jnp.broadcast_to(sel[None], (peers,) + sel.shape)
    recv = lax.all_to_all(rep, axis, 0, 0, tiled=False)
    return join_pieces(recv, BLOCK_GRID)


def cut_windows(blocks, offsets, taps, span, phases):
    batches, per_batch = offsets.shape
    _, width, samples = blocks.shape
    steps = span // phases
    lag = jnp.arange(span, dtype=offsets.dtype).reshape(steps, phases)
    idx = offsets[:, :, None, None] + lag[None, None]
    hot = (jnp.arange(samples, dtype=offsets.dtype) == idx[..., None]) & (lag[None, None, :, :, None] < taps)
    hot = hot.astype(blocks.dtype)
    cut = jnp.einsum("bkips,bcs->ibkpc", hot, blocks, preferred_element_type=jnp.float32).astype(blocks.dtype)
    return cut.reshape(steps, batches * per_batch * phases, width)


def window_norms(blocks, offsets, taps):
    floats = blocks.astype(jnp.float32)
    column = jnp.sum(floats * floats, axis=1)
    samples = blocks.shape[2]
    at = jnp.arange(samples, dtype=offsets.dtype)
    inside = (at >= offsets[:, :, None]) & (at < offsets[:, :, None] + taps)
    return jnp.sum(jnp.where(inside, column[:, None, :], 0.0), axis=2).reshape(-1)


def chan_sum(x, axis):
    peers = lax.axis_size(axis)
    pieces = dense_pieces(x, SUM_GRID)
    got = lax.all_to_all(pieces, axis, 0, 0, tiled=False)
    mine = jnp.sum(got, axis=0)
    rep = jnp.broadcast_to(mine[None], (peers,) + mine.shape)
    back = lax.all_to_all(rep, axis, 0, 0, tiled=False)
    return join_pieces(back, SUM_GRID)


def correlate(extended, weights, phases, count, samples):
    out = lax.conv_general_dilated(
        extended[None], weights, (1,), "VALID", rhs_dilation=(phases,),
        dimension_numbers=("NCH", "HOI", "NCH"), preferred_element_type=jnp.float32,
    )[0]
    out = out.reshape(count, phases, out.shape[-1])
    corr = out[:, 0, :samples]
    for p in range(1, phases):
        corr = corr + out[:, p, p : p + samples]
    return corr


def on_device(record, owner, offsets):
    width, samples = record.shape
    batches, per_batch = offsets.shape
    taps = L
    templates = batches * per_batch
    phases = PHASES
    span = -(-taps // phases) * phases
    rim = from_behind(record[:, : taps - 1], "tm", -1)
    rim, record = lax.optimization_barrier((rim, record))
    extended = jnp.concatenate(
        [record, rim, jnp.zeros((width, span - taps), record.dtype)], axis=1
    )
    widened = extended[:, : samples + taps - 1].astype(jnp.float32)
    squares = jnp.sum(widened * widened, axis=0)
    running = jnp.concatenate([jnp.zeros((1,), jnp.float32), jnp.cumsum(squares)])
    energy_part = running[taps : taps + samples] - running[:samples]
    sel = scatter_owners(record, owner, "tm")
    step = batches // STAGES
    corrs = []
    norms = []
    for g in range(STAGES):
        part = slice(g * step, (g + 1) * step)
        blocks = gather_blocks(sel[part], "tm", (width, samples))
        weights = cut_windows(blocks, offsets[part], taps, span, phases)
        corrs.append(correlate(extended, weights, phases, step * per_batch, samples))
        norms.append(window_norms(blocks, offsets[part], taps))
    rows = 80
    packed = jnp.zeros((rows, samples), jnp.float32)
    packed = packed.at[:templates].set(jnp.concatenate(corrs, axis=0))
    packed = packed.at[templates].set(energy_part)
    packed = packed.at[templates + 1, :templates].set(jnp.concatenate(norms))
    total = chan_sum(packed, "chan")
    corr = total[:templates]
    energy = total[templates]
    tnorm = total[templates + 1, :templates]
    score = corr / jnp.sqrt((energy[None, :] + 1e-05) * tnorm[:, None])
    return score.reshape(batches, per_batch, samples)


def solution(mesh):
    in_specs = (P("chan", "tm"), P(), P())
    out_specs = P(None, None, "tm")
    return jax.shard_map(
        on_device, mesh=mesh, in_specs=in_specs, out_specs=out_specs, check_vma=False
    )
```

```python
import jax
import jax.numpy as jnp
from jax import lax
from jax.sharding import PartitionSpec as P

L = 100
PHASES = 4
STAGES = 1
BLOCK_GRID = (4, 4)
SUM_GRID = (2, 8)


def from_behind(value, axis, by):
    peers = lax.axis_size(axis)
    pairs = [(i, i + by) for i in range(peers) if 0 <= i + by < peers]
    return lax.ppermute(value, axis, pairs)


def dense_pieces(block, across):
    down = block.shape[0] // across[0]
    wide = block.shape[1] // across[1]
    grid = block.reshape(across[0], down, across[1], wide)
    return jnp.transpose(grid, (0, 2, 1, 3)).reshape(across[0] * across[1], down, wide)


def join_pieces(pieces, across):
    _, *middle, down, wide = pieces.shape
    grid = pieces.reshape(across[0], across[1], *middle, down, wide)
    lead = len(middle)
    order = tuple(range(2, 2 + lead)) + (0, 2 + lead, 1, 3 + lead)
    return jnp.transpose(grid, order).reshape(*middle, across[0] * down, across[1] * wide)


def scatter_owners(record, owner, axis):
    pieces = dense_pieces(record, BLOCK_GRID)
    got = lax.all_to_all(pieces, axis, 0, 0, tiled=False)
    return jnp.stack([lax.dynamic_index_in_dim(got, owner[b], 0, keepdims=False) for b in range(owner.shape[0])])


def gather_blocks(sel, axis, shape):
    peers = lax.axis_size(axis)
    rep = jnp.broadcast_to(sel[None], (peers,) + sel.shape)
    recv = lax.all_to_all(rep, axis, 0, 0, tiled=False)
    return join_pieces(recv, BLOCK_GRID)


def cut_windows(blocks, offsets, taps, span, phases):
    batches, per_batch = offsets.shape
    _, width, samples = blocks.shape
    steps = span // phases
    lag = jnp.arange(span, dtype=offsets.dtype).reshape(steps, phases)
    idx = offsets[:, :, None, None] + lag[None, None]
    hot = (jnp.arange(samples, dtype=offsets.dtype) == idx[..., None]) & (lag[None, None, :, :, None] < taps)
    hot = hot.astype(blocks.dtype)
    cut = jnp.einsum("bkips,bcs->ibkpc", hot, blocks, preferred_element_type=jnp.float32).astype(blocks.dtype)
    return cut.reshape(steps, batches * per_batch * phases, width)


def window_norms(blocks, offsets, taps):
    floats = blocks.astype(jnp.float32)
    column = jnp.sum(floats * floats, axis=1)
    samples = blocks.shape[2]
    at = jnp.arange(samples, dtype=offsets.dtype)
    inside = (at >= offsets[:, :, None]) & (at < offsets[:, :, None] + taps)
    return jnp.sum(jnp.where(inside, column[:, None, :], 0.0), axis=2).reshape(-1)


def chan_sum(x, axis):
    peers = lax.axis_size(axis)
    pieces = dense_pieces(x, SUM_GRID)
    got = lax.all_to_all(pieces, axis, 0, 0, tiled=False)
    mine = jnp.sum(got, axis=0)
    rep = jnp.broadcast_to(mine[None], (peers,) + mine.shape)
    back = lax.all_to_all(rep, axis, 0, 0, tiled=False)
    return join_pieces(back, SUM_GRID)


def correlate(extended, weights, phases, count, samples):
    out = lax.conv_general_dilated(
        extended[None], weights, (1,), "VALID", rhs_dilation=(phases,),
        dimension_numbers=("NCH", "HOI", "NCH"), preferred_element_type=jnp.float32,
    )[0]
    out = out.reshape(count, phases, out.shape[-1])
    corr = out[:, 0, :samples]
    for p in range(1, phases):
        corr = corr + out[:, p, p : p + samples]
    return corr


def on_device(record, owner, offsets):
    width, samples = record.shape
    batches, per_batch = offsets.shape
    taps = L
    templates = batches * per_batch
    phases = PHASES
    span = -(-taps // phases) * phases
    rim = from_behind(record[:, : taps - 1], "tm", -1)
    sel = scatter_owners(record, owner, "tm")
    rim, sel = lax.optimization_barrier((rim, sel))
    extended = jnp.concatenate(
        [record, rim, jnp.zeros((width, span - taps), record.dtype)], axis=1
    )
    widened = extended[:, : samples + taps - 1].astype(jnp.float32)
    squares = jnp.sum(widened * widened, axis=0)
    running = jnp.concatenate([jnp.zeros((1,), jnp.float32), jnp.cumsum(squares)])
    energy_part = running[taps : taps + samples] - running[:samples]
    step = batches // STAGES
    corrs = []
    norms = []
    for g in range(STAGES):
        part = slice(g * step, (g + 1) * step)
        blocks = gather_blocks(sel[part], "tm", (width, samples))
        weights = cut_windows(blocks, offsets[part], taps, span, phases)
        corrs.append(correlate(extended, weights, phases, step * per_batch, samples))
        norms.append(window_norms(blocks, offsets[part], taps))
    rows = 80
    packed = jnp.zeros((rows, samples), jnp.float32)
    packed = packed.at[:templates].set(jnp.concatenate(corrs, axis=0))
    packed = packed.at[templates].set(energy_part)
    packed = packed.at[templates + 1, :templates].set(jnp.concatenate(norms))
    total = chan_sum(packed, "chan")
    corr = total[:templates]
    energy = total[templates]
    tnorm = total[templates + 1, :templates]
    score = corr / jnp.sqrt((energy[None, :] + 1e-05) * tnorm[:, None])
    return score.reshape(batches, per_batch, samples)


def solution(mesh):
    in_specs = (P("chan", "tm"), P(), P())
    out_specs = P(None, None, "tm")
    return jax.shard_map(
        on_device, mesh=mesh, in_specs=in_specs, out_specs=out_specs, check_vma=False
    )
```

```python
import jax
import jax.numpy as jnp
from jax import lax
from jax.sharding import PartitionSpec as P

L = 100
PHASES = 4
STAGES = 1
BLOCK_GRID = (2, 8)
SUM_GRID = (2, 8)


def from_behind(value, axis, by):
    peers = lax.axis_size(axis)
    pairs = [(i, i + by) for i in range(peers) if 0 <= i + by < peers]
    return lax.ppermute(value, axis, pairs)


def dense_pieces(block, across):
    down = block.shape[0] // across[0]
    wide = block.shape[1] // across[1]
    grid = block.reshape(across[0], down, across[1], wide)
    return jnp.transpose(grid, (0, 2, 1, 3)).reshape(across[0] * across[1], down, wide)


def join_pieces(pieces, across):
    _, *middle, down, wide = pieces.shape
    grid = pieces.reshape(across[0], across[1], *middle, down, wide)
    lead = len(middle)
    order = tuple(range(2, 2 + lead)) + (0, 2 + lead, 1, 3 + lead)
    return jnp.transpose(grid, order).reshape(*middle, across[0] * down, across[1] * wide)


def scatter_owners(record, owner, axis):
    pieces = dense_pieces(record, BLOCK_GRID)
    got = lax.all_to_all(pieces, axis, 0, 0, tiled=False)
    return jnp.stack([lax.dynamic_index_in_dim(got, owner[b], 0, keepdims=False) for b in range(owner.shape[0])])


def gather_blocks(sel, axis, shape):
    peers = lax.axis_size(axis)
    rep = jnp.broadcast_to(sel[None], (peers,) + sel.shape)
    recv = lax.all_to_all(rep, axis, 0, 0, tiled=False)
    return join_pieces(recv, BLOCK_GRID)


def cut_windows(blocks, offsets, taps, span, phases):
    batches, per_batch = offsets.shape
    _, width, samples = blocks.shape
    steps = span // phases
    lag = jnp.arange(span, dtype=offsets.dtype).reshape(steps, phases)
    idx = offsets[:, :, None, None] + lag[None, None]
    hot = (jnp.arange(samples, dtype=offsets.dtype) == idx[..., None]) & (lag[None, None, :, :, None] < taps)
    hot = hot.astype(blocks.dtype)
    cut = jnp.einsum("bkips,bcs->ibkpc", hot, blocks, preferred_element_type=jnp.float32).astype(blocks.dtype)
    return cut.reshape(steps, batches * per_batch * phases, width)


def window_norms(blocks, offsets, taps):
    floats = blocks.astype(jnp.float32)
    column = jnp.sum(floats * floats, axis=1)
    samples = blocks.shape[2]
    at = jnp.arange(samples, dtype=offsets.dtype)
    inside = (at >= offsets[:, :, None]) & (at < offsets[:, :, None] + taps)
    return jnp.sum(jnp.where(inside, column[:, None, :], 0.0), axis=2).reshape(-1)


def chan_sum(x, axis):
    peers = lax.axis_size(axis)
    pieces = dense_pieces(x, SUM_GRID)
    got = lax.all_to_all(pieces, axis, 0, 0, tiled=False)
    mine = jnp.sum(got, axis=0)
    rep = jnp.broadcast_to(mine[None], (peers,) + mine.shape)
    back = lax.all_to_all(rep, axis, 0, 0, tiled=False)
    return join_pieces(back, SUM_GRID)


def correlate(extended, weights, phases, count, samples):
    out = lax.conv_general_dilated(
        extended[None], weights, (1,), "VALID", rhs_dilation=(phases,),
        dimension_numbers=("NCH", "HOI", "NCH"), preferred_element_type=jnp.float32,
    )[0]
    out = out.reshape(count, phases, out.shape[-1])
    corr = out[:, 0, :samples]
    for p in range(1, phases):
        corr = corr + out[:, p, p : p + samples]
    return corr


def on_device(record, owner, offsets):
    width, samples = record.shape
    batches, per_batch = offsets.shape
    taps = L
    templates = batches * per_batch
    phases = PHASES
    span = -(-taps // phases) * phases
    rim = from_behind(record[:, : taps - 1], "tm", -1)
    sel = scatter_owners(record, owner, "tm")
    rim, sel = lax.optimization_barrier((rim, sel))
    extended = jnp.concatenate(
        [record, rim, jnp.zeros((width, span - taps), record.dtype)], axis=1
    )
    widened = extended[:, : samples + taps - 1].astype(jnp.float32)
    squares = jnp.sum(widened * widened, axis=0)
    running = jnp.concatenate([jnp.zeros((1,), jnp.float32), jnp.cumsum(squares)])
    energy_part = running[taps : taps + samples] - running[:samples]
    step = batches // STAGES
    corrs = []
    norms = []
    for g in range(STAGES):
        part = slice(g * step, (g + 1) * step)
        blocks = gather_blocks(sel[part], "tm", (width, samples))
        weights = cut_windows(blocks, offsets[part], taps, span, phases)
        corrs.append(correlate(extended, weights, phases, step * per_batch, samples))
        norms.append(window_norms(blocks, offsets[part], taps))
    rows = 80
    packed = jnp.zeros((rows, samples), jnp.float32)
    packed = packed.at[:templates].set(jnp.concatenate(corrs, axis=0))
    packed = packed.at[templates].set(energy_part)
    packed = packed.at[templates + 1, :templates].set(jnp.concatenate(norms))
    total = chan_sum(packed, "chan")
    corr = total[:templates]
    energy = total[templates]
    tnorm = total[templates + 1, :templates]
    score = corr / jnp.sqrt((energy[None, :] + 1e-05) * tnorm[:, None])
    return score.reshape(batches, per_batch, samples)


def solution(mesh):
    in_specs = (P("chan", "tm"), P(), P())
    out_specs = P(None, None, "tm")
    return jax.shard_map(
        on_device, mesh=mesh, in_specs=in_specs, out_specs=out_specs, check_vma=False
    )
```

```python
import jax
import jax.numpy as jnp
from jax import lax
from jax.sharding import PartitionSpec as P

L = 100
PHASES = 4
STAGES = 1
BLOCK_GRID = (2, 8)
SUM_GRID = (2, 8)


def from_behind(value, axis, by):
    peers = lax.axis_size(axis)
    pairs = [(i, i + by) for i in range(peers) if 0 <= i + by < peers]
    return lax.ppermute(value, axis, pairs)


def dense_pieces(block, across):
    down = block.shape[0] // across[0]
    wide = block.shape[1] // across[1]
    grid = block.reshape(across[0], down, across[1], wide)
    return jnp.transpose(grid, (0, 2, 1, 3)).reshape(across[0] * across[1], down, wide)


def join_pieces(pieces, across):
    _, *middle, down, wide = pieces.shape
    grid = pieces.reshape(across[0], across[1], *middle, down, wide)
    lead = len(middle)
    order = tuple(range(2, 2 + lead)) + (0, 2 + lead, 1, 3 + lead)
    return jnp.transpose(grid, order).reshape(*middle, across[0] * down, across[1] * wide)


def scatter_owners(record, owner, axis):
    pieces = dense_pieces(record, BLOCK_GRID)
    got = lax.all_to_all(pieces, axis, 0, 0, tiled=False)
    return jnp.stack([lax.dynamic_index_in_dim(got, owner[b], 0, keepdims=False) for b in range(owner.shape[0])])


def gather_blocks(sel, axis, shape):
    peers = lax.axis_size(axis)
    rep = jnp.broadcast_to(sel[None], (peers,) + sel.shape)
    recv = lax.all_to_all(rep, axis, 0, 0, tiled=False)
    return join_pieces(recv, BLOCK_GRID)


def cut_windows(blocks, offsets, taps, span, phases):
    batches, per_batch = offsets.shape
    _, width, samples = blocks.shape
    steps = span // phases
    lag = jnp.arange(span, dtype=offsets.dtype).reshape(steps, phases)
    idx = offsets[:, :, None, None] + lag[None, None]
    hot = (jnp.arange(samples, dtype=offsets.dtype) == idx[..., None]) & (lag[None, None, :, :, None] < taps)
    hot = hot.astype(blocks.dtype)
    cut = jnp.einsum("bcs,bkips->ibkpc", blocks, hot, preferred_element_type=jnp.float32).astype(blocks.dtype)
    return cut.reshape(steps, batches * per_batch * phases, width)


def window_norms(blocks, offsets, taps):
    floats = blocks.astype(jnp.float32)
    column = jnp.sum(floats * floats, axis=1)
    samples = blocks.shape[2]
    at = jnp.arange(samples, dtype=offsets.dtype)
    inside = (at >= offsets[:, :, None]) & (at < offsets[:, :, None] + taps)
    return jnp.sum(jnp.where(inside, column[:, None, :], 0.0), axis=2).reshape(-1)


def chan_sum(x, axis):
    peers = lax.axis_size(axis)
    pieces = dense_pieces(x, SUM_GRID)
    got = lax.all_to_all(pieces, axis, 0, 0, tiled=False)
    mine = jnp.sum(got, axis=0)
    rep = jnp.broadcast_to(mine[None], (peers,) + mine.shape)
    back = lax.all_to_all(rep, axis, 0, 0, tiled=False)
    return join_pieces(back, SUM_GRID)


def correlate(extended, weights, phases, count, samples):
    out = lax.conv_general_dilated(
        extended[None], weights, (1,), "VALID", rhs_dilation=(phases,),
        dimension_numbers=("NCH", "HOI", "NCH"), preferred_element_type=jnp.float32,
    )[0]
    out = out.reshape(count, phases, out.shape[-1])
    corr = out[:, 0, :samples]
    for p in range(1, phases):
        corr = corr + out[:, p, p : p + samples]
    return corr


def on_device(record, owner, offsets):
    width, samples = record.shape
    batches, per_batch = offsets.shape
    taps = L
    templates = batches * per_batch
    phases = PHASES
    span = -(-taps // phases) * phases
    lane = 128
    rim = from_behind(record[:, : -(-(taps - 1) // lane) * lane], "tm", -1)
    sel = scatter_owners(record, owner, "tm")
    rim, sel = lax.optimization_barrier((rim, sel))
    rim = rim[:, : taps - 1]
    extended = jnp.concatenate(
        [record, rim, jnp.zeros((width, span - taps), record.dtype)], axis=1
    )
    widened = extended[:, : samples + taps - 1].astype(jnp.float32)
    squares = jnp.sum(widened * widened, axis=0)
    running = jnp.concatenate([jnp.zeros((1,), jnp.float32), jnp.cumsum(squares)])
    energy_part = running[taps : taps + samples] - running[:samples]
    step = batches // STAGES
    corrs = []
    norms = []
    for g in range(STAGES):
        part = slice(g * step, (g + 1) * step)
        blocks = gather_blocks(sel[part], "tm", (width, samples))
        weights = cut_windows(blocks, offsets[part], taps, span, phases)
        corrs.append(correlate(extended, weights, phases, step * per_batch, samples))
        norms.append(window_norms(blocks, offsets[part], taps))
    rows = 80
    packed = jnp.zeros((rows, samples), jnp.float32)
    packed = packed.at[:templates].set(jnp.concatenate(corrs, axis=0))
    packed = packed.at[templates].set(energy_part)
    packed = packed.at[templates + 1, :templates].set(jnp.concatenate(norms))
    total = chan_sum(packed, "chan")
    corr = total[:templates]
    energy = total[templates]
    tnorm = total[templates + 1, :templates]
    score = corr / jnp.sqrt((energy[None, :] + 1e-05) * tnorm[:, None])
    return score.reshape(batches, per_batch, samples)


def solution(mesh):
    in_specs = (P("chan", "tm"), P(), P())
    out_specs = P(None, None, "tm")
    return jax.shard_map(
        on_device, mesh=mesh, in_specs=in_specs, out_specs=out_specs, check_vma=False
    )
```
